32 devices in a mesh: grp: 2 (over y), tm: 4 (over z), col: 4 (over x, core).
Axes of the slice: x: 2, y: 2, z: 4, core: 2. Of those that a mesh axis runs over, the one named last changes fastest.
Arguments:
- amplitudes: float32 [8, 8], P('grp', 'tm'), parts along dimension 0, may hold values from -1 to 1
- drift: float32 [2, 256, 256], replicated, may hold values from -0.1875 to 0.1875
- controls: float32 [4, 2, 256, 256], replicated, may hold values from -0.1875 to 0.1875
- target: float32 [4, 256, 256], P('grp'), parts along dimension 0, may hold values from -0.25 to 0.25
Outputs:
- gradient: float32 [8, 8], P('grp', 'tm'), parts along dimension 0
- propagators: float32 [16, 2, 256, 256], P(('grp', 'tm'), None, None, 'col'), parts along dimension 0
The draws below stay inside these ranges and needn't reach their ends.
There are 2 independent parts, one for each index of `grp`. The reference program is written for one: setup_inputs(seed, part) draws one part's arguments, and reference() takes and returns one part's arrays. A program takes and returns all parts, laid end to end along the dimension named above; an argument that names none is the same for every part. Nothing has to cross between parts.
All inputs are finite; a program needn't handle non-finite values.
Results may differ from the reference program's by a relative error of at most 0.0003.
Values sent between devices are 32-bit elements; how exact they have to be, the bound alone decides.
No kernel may reach another device: no remote copies, remote signals or barrier semaphores. Data moves between devices by JAX's collectives and lax.ppermute only.
A program may use at most 64 MiB of HBM per device.

```python
import jax
import jax.numpy as jnp
from jax import lax

L = 256
NCTRL = 4
TAYLOR = 8
SLICES = 8


def level_of(own_key, shape, split, smallest, top_value):
    level = 1.0
    for position, blocks in split:
        draws = jax.random.uniform(jax.random.fold_in(jax.random.fold_in(own_key, 6), position), (blocks,), jnp.float32, smallest / len(split), top_value / len(split))
        level = level * jnp.repeat(jnp.exp(draws), shape[position] // blocks).reshape((-1,) + (1,) * (len(shape) - 1 - position))
    return level


def bell_draw(stream_key, shape, deviation, limit, held_as=jnp.bfloat16):
    array = deviation * jax.random.normal(stream_key, shape, jnp.float32)
    return jnp.clip(array, min=-limit, max=limit).astype(held_as)


def setup_inputs(seed: int = 0, part: int = 0) -> dict:
    keys = jax.random.split(jax.random.key(seed), 5)
    part_splits = jax.random.split(jax.random.fold_in(keys[4], part), 5)
    amplitudes = jnp.clip(jax.random.uniform(part_splits[0], (NCTRL, SLICES), jnp.float32, -1.0, 1.0) * level_of(part_splits[0], (NCTRL, SLICES), ((1, 4),), -0.4, 0.0), -1.0, 1.0)
    drift = bell_draw(keys[1], (2, L, L), (4 * L) ** -0.5, 0.1875, jnp.float32)
    controls = bell_draw(keys[2], (NCTRL, 2, L, L), (4 * L) ** -0.5, 0.1875, jnp.float32)
    target = bell_draw(part_splits[3], (2, L, L), (2 * L) ** -0.5, 0.25, jnp.float32)
    return {"amplitudes": amplitudes, "drift": drift, "controls": controls, "target": target}


exact_mode = lax.Precision.HIGHEST


def complex_product(multiplier, multiplicand):
    real_one = jnp.dot(multiplier[0], multiplicand[0], precision=exact_mode)
    real_two = jnp.dot(multiplier[1], multiplicand[1], precision=exact_mode)
    imag_one = jnp.dot(multiplier[0], multiplicand[1], precision=exact_mode)
    imag_two = jnp.dot(multiplier[1], multiplicand[0], precision=exact_mode)
    return (real_one - real_two, imag_one + imag_two)


def reference(amplitudes, drift, controls, target):
    drift_real = 0.5 * (drift[0] + drift[0].T)
    drift_imag = 0.5 * (drift[1] - drift[1].T)
    control_real = 0.5 * (controls[:, 0] + jnp.swapaxes(controls[:, 0], 1, 2))
    control_imag = 0.5 * (controls[:, 1] - jnp.swapaxes(controls[:, 1], 1, 2))
    identity_full = jnp.eye(L, dtype=jnp.float32)
    zero_full = jnp.zeros((L, L), jnp.float32)

    def advance(previous, drives):
        ham_real = drift_real + jnp.einsum("c,cij->ij", drives, control_real, precision=exact_mode)
        ham_imag = drift_imag + jnp.einsum("c,cij->ij", drives, control_imag, precision=exact_mode)
        series_real, series_imag = identity_full, zero_full
        for order in range(TAYLOR, 0, -1):
            prod_real, prod_imag = complex_product((ham_real, ham_imag), (series_real, series_imag))
            series_real = identity_full + prod_imag / order
            series_imag = -prod_real / order
        nxt = complex_product((series_real, series_imag), previous)
        return nxt, jnp.stack([nxt[0], nxt[1]])

    final_pair, states = lax.scan(advance, (identity_full, zero_full), amplitudes.T)
    total_real, total_imag = final_pair
    correlation_real = jnp.sum(target[0] * total_real + target[1] * total_imag)
    correlation_imag = jnp.sum(target[0] * total_imag - target[1] * total_real)
    mat_real = jnp.dot(target[0].T, total_real, precision=exact_mode) + jnp.dot(target[1].T, total_imag, precision=exact_mode)
    mat_imag = jnp.dot(target[0].T, total_imag, precision=exact_mode) - jnp.dot(target[1].T, total_real, precision=exact_mode)

    def slice_terms(state):
        state_real, state_imag = state[0], state[1]
        costate_real = jnp.dot(state_real, mat_real.T, precision=exact_mode) + jnp.dot(state_imag, mat_imag.T, precision=exact_mode)
        costate_imag = jnp.dot(state_imag, mat_real.T, precision=exact_mode) - jnp.dot(state_real, mat_imag.T, precision=exact_mode)
        apply_real = jnp.einsum("cij,jk->cik", control_real, state_real, precision=exact_mode) - jnp.einsum("cij,jk->cik", control_imag, state_imag, precision=exact_mode)
        apply_imag = jnp.einsum("cij,jk->cik", control_real, state_imag, precision=exact_mode) + jnp.einsum("cij,jk->cik", control_imag, state_real, precision=exact_mode)
        trace_real = jnp.sum(apply_real * costate_real[None] + apply_imag * costate_imag[None], axis=(1, 2))
        trace_imag = jnp.sum(apply_imag * costate_real[None] - apply_real * costate_imag[None], axis=(1, 2))
        return correlation_real * trace_imag - correlation_imag * trace_real

    per_slice = lax.map(slice_terms, states)
    return (per_slice.T, states)
```

```python
import jax
import jax.numpy as jnp
from jax import lax
from jax.sharding import PartitionSpec as P

TAYLOR = 8

fast_mode = lax.Precision.HIGHEST


def mm(left, right):
    return jnp.matmul(left, right, precision=fast_mode)


def mm_nt(left, right):
    return jnp.einsum("...ij,...kj->...ik", left, right, precision=fast_mode)


def mm_tn(left, right):
    return jnp.einsum("...ji,...jk->...ik", left, right, precision=fast_mode)


def cmul(a, b):
    ar, ai = a[..., 0, :, :], a[..., 1, :, :]
    br, bi = b[..., 0, :, :], b[..., 1, :, :]
    return jnp.stack([mm(ar, br) - mm(ai, bi), mm(ar, bi) + mm(ai, br)], -3)


def cmul_adjoint_right(a, b):
    ar, ai = a[..., 0, :, :], a[..., 1, :, :]
    br, bi = b[..., 0, :, :], b[..., 1, :, :]
    return jnp.stack([mm_nt(ar, br) + mm_nt(ai, bi), mm_nt(ai, br) - mm_nt(ar, bi)], -3)


def cmul_adjoint_left(a, b):
    ar, ai = a[..., 0, :, :], a[..., 1, :, :]
    br, bi = b[..., 0, :, :], b[..., 1, :, :]
    return jnp.stack([mm_tn(ar, br) + mm_tn(ai, bi), mm_tn(ar, bi) - mm_tn(ai, br)], -3)


def taylor_propagators(ham):
    size = ham.shape[-1]
    eye = jnp.eye(size, dtype=jnp.float32)
    gen = jnp.stack([ham[:, 1], -ham[:, 0]], 1)
    gen2 = cmul(gen, gen)
    both = cmul(jnp.stack([gen, gen2], 0), gen2[None])
    gen3, gen4 = both[0], both[1]
    coef = [1.0]
    for order in range(1, TAYLOR + 1):
        coef.append(coef[-1] / order)
    low = coef[1] * gen + coef[2] * gen2 + coef[3] * gen3
    low = low.at[:, 0].add(coef[0] * eye)
    high = coef[5] * gen + coef[6] * gen2 + coef[7] * gen3 + coef[8] * gen4
    high = high.at[:, 0].add(coef[4] * eye)
    return low + cmul(gen4, high)


def shards(amplitudes, drift, controls, target):
    size = drift.shape[-1]
    tm_count = lax.axis_size("tm")
    tm_index = lax.axis_index("tm")
    col_count = lax.axis_size("col")
    col_width = size // col_count
    col_start = lax.axis_index("col") * col_width
    local_count = amplitudes.shape[1]
    exact = lax.Precision.HIGHEST

    drift_h = jnp.stack([0.5 * (drift[0] + drift[0].T), 0.5 * (drift[1] - drift[1].T)])
    control_h = jnp.stack(
        [
            0.5 * (controls[:, 0] + jnp.swapaxes(controls[:, 0], 1, 2)),
            0.5 * (controls[:, 1] - jnp.swapaxes(controls[:, 1], 1, 2)),
        ],
        1,
    )
    ham = drift_h[None] + jnp.einsum("ck,cxij->kxij", amplitudes, control_h, precision=exact)
    steps = taylor_propagators(ham)

    running = [steps[0]]
    for position in range(1, local_count):
        running.append(cmul(steps[position][None], running[-1][None])[0])
    pieces = lax.all_gather(running[-1], "tm")

    eye = jnp.eye(size, dtype=jnp.float32)
    start_full = jnp.stack([eye, jnp.zeros_like(eye)])
    if tm_count <= 8:
        scan = pieces
        shift = 1
        while shift < tm_count:
            later = cmul(scan[shift:], scan[:-shift])
            scan = jnp.concatenate([scan[:shift], later], 0)
            shift *= 2
        final_state = scan[-1]
        earlier = lax.dynamic_index_in_dim(scan, jnp.maximum(tm_index - 1, 0), 0, keepdims=False)
        prefix = jnp.where(tm_index == 0, start_full, earlier)
    else:

        def lap(carry, piece):
            total, prefix, position = carry
            prefix = jnp.where(position == tm_index, total, prefix)
            total = cmul(piece[None], total[None])[0]
            return (total, prefix, position + 1), None

        (final_state, prefix, _), _ = lax.scan(lap, (start_full, start_full, 0), pieces)
    states = cmul(jnp.stack(running, 0), prefix[None])

    correlation_real = jnp.sum(target[0] * final_state[0] + target[1] * final_state[1])
    correlation_imag = jnp.sum(target[0] * final_state[1] - target[1] * final_state[0])
    overlap = cmul_adjoint_left(target, final_state)
    weighted = cmul_adjoint_right(cmul(states, overlap[None]), states)
    control_real = control_h[:, 0][:, None]
    control_imag = control_h[:, 1][:, None]
    trace_real = jnp.sum(control_real * weighted[None, :, 0] + control_imag * weighted[None, :, 1], axis=(2, 3))
    trace_imag = jnp.sum(control_real * weighted[None, :, 1] - control_imag * weighted[None, :, 0], axis=(2, 3))
    gradient = correlation_real * trace_imag - correlation_imag * trace_real
    propagators = lax.dynamic_slice_in_dim(states, col_start, col_width, 3)
    return (gradient, propagators)


def solution(mesh):
    in_specs = (P("grp", "tm"), P(), P(), P("grp", None, None))
    out_specs = (P("grp", "tm"), P(("grp", "tm"), None, None, "col"))
    return jax.shard_map(shards, mesh=mesh, in_specs=in_specs, out_specs=out_specs, check_vma=False)
```

```python
import jax
import jax.numpy as jnp
from jax import lax
from jax.sharding import PartitionSpec as P

TAYLOR = 8

fast_mode = lax.Precision.HIGHEST


def mm(left, right):
    return jnp.matmul(left, right, precision=fast_mode)


def mm_nt(left, right):
    return jnp.einsum("...ij,...kj->...ik", left, right, precision=fast_mode)


def mm_tn(left, right):
    return jnp.einsum("...ji,...jk->...ik", left, right, precision=fast_mode)


def cmul(a, b):
    size = a.shape[-2]
    stacked = a.reshape(a.shape[:-3] + (2 * size, a.shape[-1]))
    with_real = mm(stacked, b[..., 0, :, :])
    with_imag = mm(stacked, b[..., 1, :, :])
    real = with_real[..., :size, :] - with_imag[..., size:, :]
    imag = with_imag[..., :size, :] + with_real[..., size:, :]
    return jnp.stack([real, imag], -3)


def cmul_adjoint_right(a, b):
    size = a.shape[-2]
    stacked = a.reshape(a.shape[:-3] + (2 * size, a.shape[-1]))
    with_real = mm_nt(stacked, b[..., 0, :, :])
    with_imag = mm_nt(stacked, b[..., 1, :, :])
    real = with_real[..., :size, :] + with_imag[..., size:, :]
    imag = with_real[..., size:, :] - with_imag[..., :size, :]
    return jnp.stack([real, imag], -3)


def cmul_adjoint_left(a, b):
    ar, ai = a[..., 0, :, :], a[..., 1, :, :]
    br, bi = b[..., 0, :, :], b[..., 1, :, :]
    return jnp.stack([mm_tn(ar, br) + mm_tn(ai, bi), mm_tn(ar, bi) - mm_tn(ai, br)], -3)


def taylor_propagators(ham):
    size = ham.shape[-1]
    eye = jnp.eye(size, dtype=jnp.float32)
    gen = jnp.stack([ham[:, 1], -ham[:, 0]], 1)
    gen2 = cmul(gen, gen)
    both = cmul(jnp.stack([gen, gen2], 0), gen2[None])
    gen3, gen4 = both[0], both[1]
    coef = [1.0]
    for order in range(1, TAYLOR + 1):
        coef.append(coef[-1] / order)
    low = coef[1] * gen + coef[2] * gen2 + coef[3] * gen3
    low = low.at[:, 0].add(coef[0] * eye)
    high = coef[5] * gen + coef[6] * gen2 + coef[7] * gen3 + coef[8] * gen4
    high = high.at[:, 0].add(coef[4] * eye)
    return low + cmul(gen4, high)


def shards(amplitudes, drift, controls, target):
    size = drift.shape[-1]
    tm_count = lax.axis_size("tm")
    tm_index = lax.axis_index("tm")
    col_count = lax.axis_size("col")
    col_width = size // col_count
    col_start = lax.axis_index("col") * col_width
    local_count = amplitudes.shape[1]
    exact = lax.Precision.HIGHEST

    raw = drift[None] + jnp.sum(amplitudes[:, :, None, None, None] * controls[:, None], axis=0)
    ham = jnp.stack(
        [0.5 * (raw[:, 0] + jnp.swapaxes(raw[:, 0], 1, 2)), 0.5 * (raw[:, 1] - jnp.swapaxes(raw[:, 1], 1, 2))], 1
    )
    steps = taylor_propagators(ham)

    running = [steps[0]]
    for position in range(1, local_count):
        running.append(cmul(steps[position][None], running[-1][None])[0])
    block_total = running[-1]
    split = 2 if col_count % 2 == 0 else 1
    if split == 2:
        half = size // 2
        col_index = lax.axis_index("col")
        part = col_index % 2
        mine = lax.all_gather(lax.dynamic_slice_in_dim(block_total, part * half, half, 1), "tm")
        theirs = lax.ppermute(mine, "col", [(i, i ^ 1) for i in range(col_count)])
        upper = jnp.where(part == 0, mine, theirs)
        lower = jnp.where(part == 0, theirs, mine)
        pieces = jnp.concatenate([upper, lower], 2)
    else:
        pieces = lax.all_gather(block_total, "tm")

    eye = jnp.eye(size, dtype=jnp.float32)
    start_full = jnp.stack([eye, jnp.zeros_like(eye)])
    if tm_count <= 8:
        scan = pieces
        shift = 1
        while shift < tm_count:
            later = cmul(scan[shift:], scan[:-shift])
            scan = jnp.concatenate([scan[:shift], later], 0)
            shift *= 2
        final_state = scan[-1]
        earlier = lax.dynamic_index_in_dim(scan, jnp.maximum(tm_index - 1, 0), 0, keepdims=False)
        prefix = jnp.where(tm_index == 0, start_full, earlier)
    else:

        def lap(carry, piece):
            total, prefix, position = carry
            prefix = jnp.where(position == tm_index, total, prefix)
            total = cmul(piece[None], total[None])[0]
            return (total, prefix, position + 1), None

        (final_state, prefix, _), _ = lax.scan(lap, (start_full, start_full, 0), pieces)
    states = cmul(jnp.stack(running, 0), prefix[None])

    correlation_real = jnp.sum(target[0] * final_state[0] + target[1] * final_state[1])
    correlation_imag = jnp.sum(target[0] * final_state[1] - target[1] * final_state[0])
    overlap = cmul_adjoint_left(target, final_state)
    weighted = cmul_adjoint_right(cmul(states, overlap[None]), states)
    control_real = (0.5 * (controls[:, 0] + jnp.swapaxes(controls[:, 0], 1, 2)))[:, None]
    control_imag = (0.5 * (controls[:, 1] - jnp.swapaxes(controls[:, 1], 1, 2)))[:, None]
    trace_real = jnp.sum(control_real * weighted[None, :, 0] + control_imag * weighted[None, :, 1], axis=(2, 3))
    trace_imag = jnp.sum(control_real * weighted[None, :, 1] - control_imag * weighted[None, :, 0], axis=(2, 3))
    gradient = correlation_real * trace_imag - correlation_imag * trace_real
    propagators = lax.dynamic_slice_in_dim(states, col_start, col_width, 3)
    return (gradient, propagators)


def solution(mesh):
    in_specs = (P("grp", "tm"), P(), P(), P("grp", None, None))
    out_specs = (P("grp", "tm"), P(("grp", "tm"), None, None, "col"))
    return jax.shard_map(shards, mesh=mesh, in_specs=in_specs, out_specs=out_specs, check_vma=False)
```

```python
import jax
import jax.numpy as jnp
from jax import lax
from jax.sharding import PartitionSpec as P

TAYLOR = 8

fast_mode = lax.Precision.HIGHEST


def mm(left, right):
    return jnp.matmul(left, right, precision=fast_mode)


def mm_nt(left, right):
    return jnp.einsum("...ij,...kj->...ik", left, right, precision=fast_mode)


def mm_tn(left, right):
    return jnp.einsum("...ji,...jk->...ik", left, right, precision=fast_mode)


def cmul(a, b):
    size = a.shape[-2]
    stacked = a.reshape(a.shape[:-3] + (2 * size, a.shape[-1]))
    with_real = mm(stacked, b[..., 0, :, :])
    with_imag = mm(stacked, b[..., 1, :, :])
    real = with_real[..., :size, :] - with_imag[..., size:, :]
    imag = with_imag[..., :size, :] + with_real[..., size:, :]
    return jnp.stack([real, imag], -3)


def cmul_adjoint_right(a, b):
    size = a.shape[-2]
    stacked = a.reshape(a.shape[:-3] + (2 * size, a.shape[-1]))
    with_real = mm_nt(stacked, b[..., 0, :, :])
    with_imag = mm_nt(stacked, b[..., 1, :, :])
    real = with_real[..., :size, :] + with_imag[..., size:, :]
    imag = with_real[..., size:, :] - with_imag[..., :size, :]
    return jnp.stack([real, imag], -3)


def cmul_adjoint_left(a, b):
    ar, ai = a[..., 0, :, :], a[..., 1, :, :]
    br, bi = b[..., 0, :, :], b[..., 1, :, :]
    return jnp.stack([mm_tn(ar, br) + mm_tn(ai, bi), mm_tn(ar, bi) - mm_tn(ai, br)], -3)


def taylor_propagators(ham):
    size = ham.shape[-1]
    eye = jnp.eye(size, dtype=jnp.float32)
    gen = jnp.stack([ham[:, 1], -ham[:, 0]], 1)
    gen2 = cmul(gen, gen)
    both = cmul(jnp.stack([gen, gen2], 0), gen2[None])
    gen3, gen4 = both[0], both[1]
    coef = [1.0]
    for order in range(1, TAYLOR + 1):
        coef.append(coef[-1] / order)
    low = coef[1] * gen + coef[2] * gen2 + coef[3] * gen3
    low = low.at[:, 0].add(coef[0] * eye)
    high = coef[5] * gen + coef[6] * gen2 + coef[7] * gen3 + coef[8] * gen4
    high = high.at[:, 0].add(coef[4] * eye)
    return low + cmul(gen4, high)


def shards(amplitudes, drift, controls, target):
    size = drift.shape[-1]
    tm_count = lax.axis_size("tm")
    tm_index = lax.axis_index("tm")
    col_count = lax.axis_size("col")
    col_width = size // col_count
    col_start = lax.axis_index("col") * col_width
    local_count = amplitudes.shape[1]
    exact = lax.Precision.HIGHEST

    raw = drift[None] + jnp.sum(amplitudes[:, :, None, None, None] * controls[:, None], axis=0)
    ham = jnp.stack(
        [0.5 * (raw[:, 0] + jnp.swapaxes(raw[:, 0], 1, 2)), 0.5 * (raw[:, 1] - jnp.swapaxes(raw[:, 1], 1, 2))], 1
    )
    steps = taylor_propagators(ham)

    running = [steps[0]]
    for position in range(1, local_count):
        running.append(cmul(steps[position][None], running[-1][None])[0])
    block_total = running[-1]
    split = 2 if col_count % 2 == 0 else 1
    part = lax.axis_index("col") % split
    rows = size // split
    mine = lax.dynamic_slice_in_dim(block_total, part * rows, rows, 1)
    if tm_count <= 8:
        slots = jnp.arange(tm_count)[:, None, None, None]
        gathered = jnp.where(slots == tm_index, mine[None], jnp.zeros_like(mine)[None])
        for shift in range(1, tm_count):
            for sign in (1, -1):
                pairs = [(i, i + sign * shift) for i in range(tm_count) if 0 <= i + sign * shift < tm_count]
                moved = lax.ppermute(mine, "tm", pairs)
                gathered = jnp.where(slots == tm_index - sign * shift, moved[None], gathered)
    else:
        gathered = lax.all_gather(mine, "tm")
    if split == 2:
        theirs = lax.ppermute(gathered, "col", [(i, i ^ 1) for i in range(col_count)])
        upper = jnp.where(part == 0, gathered, theirs)
        lower = jnp.where(part == 0, theirs, gathered)
        pieces = jnp.concatenate([upper, lower], 2)
    else:
        pieces = gathered

    eye = jnp.eye(size, dtype=jnp.float32)
    start_full = jnp.stack([eye, jnp.zeros_like(eye)])
    if tm_count <= 8:
        scan = pieces
        shift = 1
        while shift < tm_count:
            later = cmul(scan[shift:], scan[:-shift])
            scan = jnp.concatenate([scan[:shift], later], 0)
            shift *= 2
        final_state = scan[-1]
        earlier = lax.dynamic_index_in_dim(scan, jnp.maximum(tm_index - 1, 0), 0, keepdims=False)
        prefix = jnp.where(tm_index == 0, start_full, earlier)
    else:

        def lap(carry, piece):
            total, prefix, position = carry
            prefix = jnp.where(position == tm_index, total, prefix)
            total = cmul(piece[None], total[None])[0]
            return (total, prefix, position + 1), None

        (final_state, prefix, _), _ = lax.scan(lap, (start_full, start_full, 0), pieces)
    states = cmul(jnp.stack(running, 0), prefix[None])

    correlation_real = jnp.sum(target[0] * final_state[0] + target[1] * final_state[1])
    correlation_imag = jnp.sum(target[0] * final_state[1] - target[1] * final_state[0])
    overlap = cmul_adjoint_left(target, final_state)
    weighted = cmul_adjoint_right(cmul(states, overlap[None]), states)
    control_real = (0.5 * (controls[:, 0] + jnp.swapaxes(controls[:, 0], 1, 2)))[:, None]
    control_imag = (0.5 * (controls[:, 1] - jnp.swapaxes(controls[:, 1], 1, 2)))[:, None]
    trace_real = jnp.sum(control_real * weighted[None, :, 0] + control_imag * weighted[None, :, 1], axis=(2, 3))
    trace_imag = jnp.sum(control_real * weighted[None, :, 1] - control_imag * weighted[None, :, 0], axis=(2, 3))
    gradient = correlation_real * trace_imag - correlation_imag * trace_real
    propagators = lax.dynamic_slice_in_dim(states, col_start, col_width, 3)
    return (gradient, propagators)


def solution(mesh):
    in_specs = (P("grp", "tm"), P(), P(), P("grp", None, None))
    out_specs = (P("grp", "tm"), P(("grp", "tm"), None, None, "col"))
    return jax.shard_map(shards, mesh=mesh, in_specs=in_specs, out_specs=out_specs, check_vma=False)
```

```python
import jax
import jax.numpy as jnp
from jax import lax
from jax.sharding import PartitionSpec as P

TAYLOR = 8

fast_mode = lax.Precision.HIGHEST
taylor_mode = lax.Precision.HIGHEST


def mm(left, right, mode=fast_mode):
    return jnp.matmul(left, right, precision=mode)


def mm_nt(left, right):
    return jnp.einsum("...ij,...kj->...ik", left, right, precision=fast_mode)


def mm_tn(left, right):
    return jnp.einsum("...ji,...jk->...ik", left, right, precision=fast_mode)


def cmul(a, b, mode=fast_mode):
    size = a.shape[-2]
    stacked = a.reshape(a.shape[:-3] + (2 * size, a.shape[-1]))
    with_real = mm(stacked, b[..., 0, :, :], mode)
    with_imag = mm(stacked, b[..., 1, :, :], mode)
    real = with_real[..., :size, :] - with_imag[..., size:, :]
    imag = with_imag[..., :size, :] + with_real[..., size:, :]
    return jnp.stack([real, imag], -3)


def cmul_adjoint_right(a, b):
    size = a.shape[-2]
    stacked = a.reshape(a.shape[:-3] + (2 * size, a.shape[-1]))
    with_real = mm_nt(stacked, b[..., 0, :, :])
    with_imag = mm_nt(stacked, b[..., 1, :, :])
    real = with_real[..., :size, :] + with_imag[..., size:, :]
    imag = with_real[..., size:, :] - with_imag[..., :size, :]
    return jnp.stack([real, imag], -3)


def cmul_adjoint_left(a, b):
    ar, ai = a[..., 0, :, :], a[..., 1, :, :]
    br, bi = b[..., 0, :, :], b[..., 1, :, :]
    return jnp.stack([mm_tn(ar, br) + mm_tn(ai, bi), mm_tn(ar, bi) - mm_tn(ai, br)], -3)


def taylor_propagators(ham):
    size = ham.shape[-1]
    eye = jnp.eye(size, dtype=jnp.float32)
    gen = jnp.stack([ham[:, 1], -ham[:, 0]], 1)
    gen2 = cmul(gen, gen, taylor_mode)
    both = cmul(jnp.stack([gen, gen2], 0), gen2[None], taylor_mode)
    gen3, gen4 = both[0], both[1]
    coef = [1.0]
    for order in range(1, TAYLOR + 1):
        coef.append(coef[-1] / order)
    low = coef[1] * gen + coef[2] * gen2 + coef[3] * gen3
    low = low.at[:, 0].add(coef[0] * eye)
    high = coef[5] * gen + coef[6] * gen2 + coef[7] * gen3 + coef[8] * gen4
    high = high.at[:, 0].add(coef[4] * eye)
    return low + cmul(gen4, high, taylor_mode)


def shards(amplitudes, drift, controls, target):
    size = drift.shape[-1]
    tm_count = lax.axis_size("tm")
    tm_index = lax.axis_index("tm")
    col_count = lax.axis_size("col")
    col_width = size // col_count
    col_start = lax.axis_index("col") * col_width
    local_count = amplitudes.shape[1]
    exact = lax.Precision.HIGHEST

    raw = drift[None] + jnp.sum(amplitudes[:, :, None, None, None] * controls[:, None], axis=0)
    ham = jnp.stack(
        [0.5 * (raw[:, 0] + jnp.swapaxes(raw[:, 0], 1, 2)), 0.5 * (raw[:, 1] - jnp.swapaxes(raw[:, 1], 1, 2))], 1
    )
    steps = taylor_propagators(ham)

    running = [steps[0]]
    for position in range(1, local_count):
        running.append(cmul(steps[position][None], running[-1][None])[0])
    block_total = running[-1]
    split = 2 if col_count % 2 == 0 else 1
    part = lax.axis_index("col") % split
    rows = size // split
    mine = lax.dynamic_slice_in_dim(block_total, part * rows, rows, 1)
    if tm_count <= 8:
        received = []
        for shift in range(1, tm_count):
            pairs = [(i, (i + shift) % tm_count) for i in range(tm_count)]
            received.append(lax.ppermute(mine, "tm", pairs))
        received = jnp.stack(received, 0)
        if split == 2:
            theirs = lax.ppermute(received, "col", [(i, i ^ 1) for i in range(col_count)])
            own_block = block_total
            received = jnp.where(
                part == 0, jnp.concatenate([received, theirs], 2), jnp.concatenate([theirs, received], 2)
            )
        else:
            own_block = block_total
        slots = jnp.arange(tm_count)[:, None, None, None]
        pieces = jnp.where(slots == tm_index, own_block[None], jnp.zeros_like(own_block)[None])
        for shift in range(1, tm_count):
            pieces = jnp.where(slots == (tm_index - shift) % tm_count, received[shift - 1][None], pieces)
    else:
        gathered = lax.all_gather(mine, "tm")
        if split == 2:
            theirs = lax.ppermute(gathered, "col", [(i, i ^ 1) for i in range(col_count)])
            upper = jnp.where(part == 0, gathered, theirs)
            lower = jnp.where(part == 0, theirs, gathered)
            pieces = jnp.concatenate([upper, lower], 2)
        else:
            pieces = gathered

    eye = jnp.eye(size, dtype=jnp.float32)
    start_full = jnp.stack([eye, jnp.zeros_like(eye)])
    if tm_count <= 8:
        scan = pieces
        shift = 1
        while shift < tm_count:
            later = cmul(scan[shift:], scan[:-shift])
            scan = jnp.concatenate([scan[:shift], later], 0)
            shift *= 2
        final_state = scan[-1]
        earlier = lax.dynamic_index_in_dim(scan, jnp.maximum(tm_index - 1, 0), 0, keepdims=False)
        prefix = jnp.where(tm_index == 0, start_full, earlier)
    else:

        def lap(carry, piece):
            total, prefix, position = carry
            prefix = jnp.where(position == tm_index, total, prefix)
            total = cmul(piece[None], total[None])[0]
            return (total, prefix, position + 1), None

        (final_state, prefix, _), _ = lax.scan(lap, (start_full, start_full, 0), pieces)
    states = cmul(jnp.stack(running, 0), prefix[None])

    correlation_real = jnp.sum(target[0] * final_state[0] + target[1] * final_state[1])
    correlation_imag = jnp.sum(target[0] * final_state[1] - target[1] * final_state[0])
    overlap = cmul_adjoint_left(target, final_state)
    weighted = cmul_adjoint_right(cmul(states, overlap[None]), states)
    control_real = (0.5 * (controls[:, 0] + jnp.swapaxes(controls[:, 0], 1, 2)))[:, None]
    control_imag = (0.5 * (controls[:, 1] - jnp.swapaxes(controls[:, 1], 1, 2)))[:, None]
    trace_real = jnp.sum(control_real * weighted[None, :, 0] + control_imag * weighted[None, :, 1], axis=(2, 3))
    trace_imag = jnp.sum(control_real * weighted[None, :, 1] - control_imag * weighted[None, :, 0], axis=(2, 3))
    gradient = correlation_real * trace_imag - correlation_imag * trace_real
    propagators = lax.dynamic_slice_in_dim(states, col_start, col_width, 3)
    return (gradient, propagators)


def solution(mesh):
    in_specs = (P("grp", "tm"), P(), P(), P("grp", None, None))
    out_specs = (P("grp", "tm"), P(("grp", "tm"), None, None, "col"))
    return jax.shard_map(shards, mesh=mesh, in_specs=in_specs, out_specs=out_specs, check_vma=False)
```

```python
import jax
import jax.numpy as jnp
from jax import lax
from jax.sharding import PartitionSpec as P

TAYLOR = 8

fast_mode = lax.Precision.HIGHEST
taylor_mode = lax.Precision.HIGHEST


def mm(left, right, mode=fast_mode):
    return jnp.matmul(left, right, precision=mode)


def mm_nt(left, right):
    return jnp.einsum("...ij,...kj->...ik", left, right, precision=fast_mode)


def mm_tn(left, right):
    return jnp.einsum("...ji,...jk->...ik", left, right, precision=fast_mode)


def cmul(a, b, mode=fast_mode):
    size = a.shape[-2]
    stacked = a.reshape(a.shape[:-3] + (2 * size, a.shape[-1]))
    with_real = mm(stacked, b[..., 0, :, :], mode)
    with_imag = mm(stacked, b[..., 1, :, :], mode)
    real = with_real[..., :size, :] - with_imag[..., size:, :]
    imag = with_imag[..., :size, :] + with_real[..., size:, :]
    return jnp.stack([real, imag], -3)


def cmul_adjoint_right(a, b):
    size = a.shape[-2]
    stacked = a.reshape(a.shape[:-3] + (2 * size, a.shape[-1]))
    with_real = mm_nt(stacked, b[..., 0, :, :])
    with_imag = mm_nt(stacked, b[..., 1, :, :])
    real = with_real[..., :size, :] + with_imag[..., size:, :]
    imag = with_real[..., size:, :] - with_imag[..., :size, :]
    return jnp.stack([real, imag], -3)


def cmul_adjoint_left(a, b):
    ar, ai = a[..., 0, :, :], a[..., 1, :, :]
    br, bi = b[..., 0, :, :], b[..., 1, :, :]
    return jnp.stack([mm_tn(ar, br) + mm_tn(ai, bi), mm_tn(ar, bi) - mm_tn(ai, br)], -3)


def taylor_propagators(ham):
    size = ham.shape[-1]
    eye = jnp.eye(size, dtype=jnp.float32)
    gen = jnp.stack([ham[:, 1], -ham[:, 0]], 1)
    gen2 = cmul(gen, gen, taylor_mode)
    both = cmul(jnp.stack([gen, gen2], 0), gen2[None], taylor_mode)
    gen3, gen4 = both[0], both[1]
    coef = [1.0]
    for order in range(1, TAYLOR + 1):
        coef.append(coef[-1] / order)
    low = coef[1] * gen + coef[2] * gen2 + coef[3] * gen3
    low = low.at[:, 0].add(coef[0] * eye)
    high = coef[5] * gen + coef[6] * gen2 + coef[7] * gen3 + coef[8] * gen4
    high = high.at[:, 0].add(coef[4] * eye)
    return low + cmul(gen4, high, taylor_mode)


def shards(amplitudes, drift, controls, target):
    size = drift.shape[-1]
    tm_count = lax.axis_size("tm")
    tm_index = lax.axis_index("tm")
    col_count = lax.axis_size("col")
    col_width = size // col_count
    col_start = lax.axis_index("col") * col_width
    local_count = amplitudes.shape[1]
    exact = lax.Precision.HIGHEST

    raw = drift[None] + jnp.sum(amplitudes[:, :, None, None, None] * controls[:, None], axis=0)
    ham = jnp.stack(
        [0.5 * (raw[:, 0] + jnp.swapaxes(raw[:, 0], 1, 2)), 0.5 * (raw[:, 1] - jnp.swapaxes(raw[:, 1], 1, 2))], 1
    )
    steps = taylor_propagators(ham)

    running = [steps[0]]
    for position in range(1, local_count):
        running.append(cmul(steps[position][None], running[-1][None])[0])
    block_total = running[-1]
    split = 2 if col_count % 2 == 0 else 1
    part = lax.axis_index("col") % split
    rows = size // split
    mine = lax.dynamic_slice_in_dim(block_total, part * rows, rows, 1)
    if tm_count <= 8:
        received = []
        for shift in range(1, tm_count):
            pairs = [(i, (i + shift) % tm_count) for i in range(tm_count)]
            received.append(lax.ppermute(mine, "tm", pairs))
        received = jnp.stack(received, 0)
        if split == 2:
            theirs = lax.ppermute(received, "col", [(i, i ^ 1) for i in range(col_count)])
            own_block = block_total
            received = jnp.where(
                part == 0, jnp.concatenate([received, theirs], 2), jnp.concatenate([theirs, received], 2)
            )
        else:
            own_block = block_total
        slots = jnp.arange(tm_count)[:, None, None, None]
        pieces = jnp.where(slots == tm_index, own_block[None], jnp.zeros_like(own_block)[None])
        for shift in range(1, tm_count):
            pieces = jnp.where(slots == (tm_index - shift) % tm_count, received[shift - 1][None], pieces)
    else:
        gathered = lax.all_gather(mine, "tm")
        if split == 2:
            theirs = lax.ppermute(gathered, "col", [(i, i ^ 1) for i in range(col_count)])
            upper = jnp.where(part == 0, gathered, theirs)
            lower = jnp.where(part == 0, theirs, gathered)
            pieces = jnp.concatenate([upper, lower], 2)
        else:
            pieces = gathered

    eye = jnp.eye(size, dtype=jnp.float32)
    start_full = jnp.stack([eye, jnp.zeros_like(eye)])
    if tm_count == 4:
        pairs = cmul(pieces[1::2], pieces[0::2])
        ends = cmul(jnp.stack([pairs[1], pieces[2]], 0), pairs[0][None])
        final_state = ends[0]
        options = jnp.stack([start_full, pieces[0], pairs[0], ends[1]], 0)
        prefix = lax.dynamic_index_in_dim(options, tm_index, 0, keepdims=False)
    elif tm_count <= 8:
        scan = pieces
        shift = 1
        while shift < tm_count:
            later = cmul(scan[shift:], scan[:-shift])
            scan = jnp.concatenate([scan[:shift], later], 0)
            shift *= 2
        final_state = scan[-1]
        earlier = lax.dynamic_index_in_dim(scan, jnp.maximum(tm_index - 1, 0), 0, keepdims=False)
        prefix = jnp.where(tm_index == 0, start_full, earlier)
    else:

        def lap(carry, piece):
            total, prefix, position = carry
            prefix = jnp.where(position == tm_index, total, prefix)
            total = cmul(piece[None], total[None])[0]
            return (total, prefix, position + 1), None

        (final_state, prefix, _), _ = lax.scan(lap, (start_full, start_full, 0), pieces)
    states = cmul(jnp.stack(running, 0), prefix[None])
    overlap = cmul_adjoint_left(target, final_state)

    correlation_real = jnp.sum(target[0] * final_state[0] + target[1] * final_state[1])
    correlation_imag = jnp.sum(target[0] * final_state[1] - target[1] * final_state[0])
    weighted = cmul_adjoint_right(cmul(states, overlap[None]), states)
    control_real = (0.5 * (controls[:, 0] + jnp.swapaxes(controls[:, 0], 1, 2)))[:, None]
    control_imag = (0.5 * (controls[:, 1] - jnp.swapaxes(controls[:, 1], 1, 2)))[:, None]
    trace_real = jnp.sum(control_real * weighted[None, :, 0] + control_imag * weighted[None, :, 1], axis=(2, 3))
    trace_imag = jnp.sum(control_real * weighted[None, :, 1] - control_imag * weighted[None, :, 0], axis=(2, 3))
    gradient = correlation_real * trace_imag - correlation_imag * trace_real
    propagators = cmul(jnp.stack(running, 0), lax.dynamic_slice_in_dim(prefix, col_start, col_width, 2)[None])
    return (gradient, propagators)


def solution(mesh):
    in_specs = (P("grp", "tm"), P(), P(), P("grp", None, None))
    out_specs = (P("grp", "tm"), P(("grp", "tm"), None, None, "col"))
    return jax.shard_map(shards, mesh=mesh, in_specs=in_specs, out_specs=out_specs, check_vma=False)
```

```python
import jax
import jax.numpy as jnp
from jax import lax
from jax.sharding import PartitionSpec as P

TAYLOR = 8

fast_mode = lax.Precision.HIGHEST
taylor_mode = lax.Precision.HIGHEST


def mm(left, right, mode=fast_mode):
    return jnp.matmul(left, right, precision=mode)


def mm_nt(left, right):
    return jnp.einsum("...ij,...kj->...ik", left, right, precision=fast_mode)


def mm_tn(left, right):
    return jnp.einsum("...ji,...jk->...ik", left, right, precision=fast_mode)


def cmul(a, b, mode=fast_mode):
    size = a.shape[-2]
    stacked = a.reshape(a.shape[:-3] + (2 * size, a.shape[-1]))
    with_real = mm(stacked, b[..., 0, :, :], mode)
    with_imag = mm(stacked, b[..., 1, :, :], mode)
    real = with_real[..., :size, :] - with_imag[..., size:, :]
    imag = with_imag[..., :size, :] + with_real[..., size:, :]
    return jnp.stack([real, imag], -3)


def cmul_adjoint_right(a, b):
    size = a.shape[-2]
    stacked = a.reshape(a.shape[:-3] + (2 * size, a.shape[-1]))
    with_real = mm_nt(stacked, b[..., 0, :, :])
    with_imag = mm_nt(stacked, b[..., 1, :, :])
    real = with_real[..., :size, :] + with_imag[..., size:, :]
    imag = with_real[..., size:, :] - with_imag[..., :size, :]
    return jnp.stack([real, imag], -3)


def cmul_adjoint_left(a, b):
    size = a.shape[-2]
    stacked = a.reshape(a.shape[:-3] + (2 * size, a.shape[-1]))
    real = mm_tn(stacked, b.reshape(b.shape[:-3] + (2 * size, b.shape[-1])))
    swapped = jnp.stack([b[..., 1, :, :], -b[..., 0, :, :]], -3)
    imag = mm_tn(stacked, swapped.reshape(b.shape[:-3] + (2 * size, b.shape[-1])))
    return jnp.stack([real, imag], -3)


def taylor_propagators(ham):
    size = ham.shape[-1]
    eye = jnp.eye(size, dtype=jnp.float32)
    gen = jnp.stack([ham[:, 1], -ham[:, 0]], 1)
    gen2 = cmul(gen, gen, taylor_mode)
    both = cmul(jnp.stack([gen, gen2], 0), gen2[None], taylor_mode)
    gen3, gen4 = both[0], both[1]
    coef = [1.0]
    for order in range(1, TAYLOR + 1):
        coef.append(coef[-1] / order)
    low = coef[1] * gen + coef[2] * gen2 + coef[3] * gen3
    low = low.at[:, 0].add(coef[0] * eye)
    high = coef[5] * gen + coef[6] * gen2 + coef[7] * gen3 + coef[8] * gen4
    high = high.at[:, 0].add(coef[4] * eye)
    return low + cmul(gen4, high, taylor_mode)


def shards(amplitudes, drift, controls, target):
    size = drift.shape[-1]
    tm_count = lax.axis_size("tm")
    tm_index = lax.axis_index("tm")
    col_count = lax.axis_size("col")
    col_width = size // col_count
    col_start = lax.axis_index("col") * col_width
    local_count = amplitudes.shape[1]
    exact = lax.Precision.HIGHEST

    raw = drift[None] + jnp.sum(amplitudes[:, :, None, None, None] * controls[:, None], axis=0)
    ham = jnp.stack(
        [0.5 * (raw[:, 0] + jnp.swapaxes(raw[:, 0], 1, 2)), 0.5 * (raw[:, 1] - jnp.swapaxes(raw[:, 1], 1, 2))], 1
    )
    steps = taylor_propagators(ham)

    running = [steps[0]]
    for position in range(1, local_count):
        running.append(cmul(steps[position][None], running[-1][None])[0])
    block_total = running[-1]
    split = 2 if col_count % 2 == 0 else 1
    part = lax.axis_index("col") % split
    rows = size // split
    mine = lax.dynamic_slice_in_dim(block_total, part * rows, rows, 1)
    if tm_count <= 8:
        received = []
        for shift in range(1, tm_count):
            pairs = [(i, (i + shift) % tm_count) for i in range(tm_count)]
            received.append(lax.ppermute(mine, "tm", pairs))
        received = jnp.stack(received, 0)
        if split == 2:
            theirs = lax.ppermute(received, "col", [(i, i ^ 1) for i in range(col_count)])
            own_block = block_total
            received = jnp.where(
                part == 0, jnp.concatenate([received, theirs], 2), jnp.concatenate([theirs, received], 2)
            )
        else:
            own_block = block_total
        slots = jnp.arange(tm_count)[:, None, None, None]
        pieces = jnp.where(slots == tm_index, own_block[None], jnp.zeros_like(own_block)[None])
        for shift in range(1, tm_count):
            pieces = jnp.where(slots == (tm_index - shift) % tm_count, received[shift - 1][None], pieces)
    else:
        gathered = lax.all_gather(mine, "tm")
        if split == 2:
            theirs = lax.ppermute(gathered, "col", [(i, i ^ 1) for i in range(col_count)])
            upper = jnp.where(part == 0, gathered, theirs)
            lower = jnp.where(part == 0, theirs, gathered)
            pieces = jnp.concatenate([upper, lower], 2)
        else:
            pieces = gathered

    eye = jnp.eye(size, dtype=jnp.float32)
    start_full = jnp.stack([eye, jnp.zeros_like(eye)])
    if tm_count == 4:
        pairs = cmul(pieces[1::2], pieces[0::2])
        ends = cmul(jnp.stack([pairs[1], pieces[2]], 0), pairs[0][None])
        final_state = ends[0]
        options = jnp.stack([start_full, pieces[0], pairs[0], ends[1]], 0)
        prefix = lax.dynamic_index_in_dim(options, tm_index, 0, keepdims=False)
    elif tm_count <= 8:
        scan = pieces
        shift = 1
        while shift < tm_count:
            later = cmul(scan[shift:], scan[:-shift])
            scan = jnp.concatenate([scan[:shift], later], 0)
            shift *= 2
        final_state = scan[-1]
        earlier = lax.dynamic_index_in_dim(scan, jnp.maximum(tm_index - 1, 0), 0, keepdims=False)
        prefix = jnp.where(tm_index == 0, start_full, earlier)
    else:

        def lap(carry, piece):
            total, prefix, position = carry
            prefix = jnp.where(position == tm_index, total, prefix)
            total = cmul(piece[None], total[None])[0]
            return (total, prefix, position + 1), None

        (final_state, prefix, _), _ = lax.scan(lap, (start_full, start_full, 0), pieces)
    states = cmul(jnp.stack(running, 0), prefix[None])
    overlap = cmul_adjoint_left(target, final_state)

    correlation_real = jnp.sum(target[0] * final_state[0] + target[1] * final_state[1])
    correlation_imag = jnp.sum(target[0] * final_state[1] - target[1] * final_state[0])
    weighted = cmul_adjoint_right(cmul(states, overlap[None]), states)
    control_real = (0.5 * (controls[:, 0] + jnp.swapaxes(controls[:, 0], 1, 2)))[:, None]
    control_imag = (0.5 * (controls[:, 1] - jnp.swapaxes(controls[:, 1], 1, 2)))[:, None]
    trace_real = jnp.sum(control_real * weighted[None, :, 0] + control_imag * weighted[None, :, 1], axis=(2, 3))
    trace_imag = jnp.sum(control_real * weighted[None, :, 1] - control_imag * weighted[None, :, 0], axis=(2, 3))
    gradient = correlation_real * trace_imag - correlation_imag * trace_real
    propagators = cmul(jnp.stack(running, 0), lax.dynamic_slice_in_dim(prefix, col_start, col_width, 2)[None])
    return (gradient, propagators)


def solution(mesh):
    in_specs = (P("grp", "tm"), P(), P(), P("grp", None, None))
    out_specs = (P("grp", "tm"), P(("grp", "tm"), None, None, "col"))
    return jax.shard_map(shards, mesh=mesh, in_specs=in_specs, out_specs=out_specs, check_vma=False)
```

```python
import jax
import jax.numpy as jnp
from jax import lax
from jax.sharding import PartitionSpec as P

TAYLOR = 8

fast_mode = lax.Precision.HIGHEST
taylor_mode = lax.Precision.HIGHEST


def mm(left, right, mode=fast_mode):
    return jnp.matmul(left, right, precision=mode)


def mm_nt(left, right):
    return jnp.einsum("...ij,...kj->...ik", left, right, precision=fast_mode)


def mm_tn(left, right):
    return jnp.einsum("...ji,...jk->...ik", left, right, precision=fast_mode)


def cmul(a, b, mode=fast_mode):
    size = a.shape[-2]
    stacked = a.reshape(a.shape[:-3] + (2 * size, a.shape[-1]))
    with_real = mm(stacked, b[..., 0, :, :], mode)
    with_imag = mm(stacked, b[..., 1, :, :], mode)
    real = with_real[..., :size, :] - with_imag[..., size:, :]
    imag = with_imag[..., :size, :] + with_real[..., size:, :]
    return jnp.stack([real, imag], -3)


def cmul_adjoint_right(a, b):
    size = a.shape[-2]
    stacked = a.reshape(a.shape[:-3] + (2 * size, a.shape[-1]))
    with_real = mm_nt(stacked, b[..., 0, :, :])
    with_imag = mm_nt(stacked, b[..., 1, :, :])
    real = with_real[..., :size, :] + with_imag[..., size:, :]
    imag = with_real[..., size:, :] - with_imag[..., :size, :]
    return jnp.stack([real, imag], -3)


def cmul_adjoint_left(a, b):
    size = a.shape[-2]
    stacked = a.reshape(a.shape[:-3] + (2 * size, a.shape[-1]))
    real = mm_tn(stacked, b.reshape(b.shape[:-3] + (2 * size, b.shape[-1])))
    swapped = jnp.stack([b[..., 1, :, :], -b[..., 0, :, :]], -3)
    imag = mm_tn(stacked, swapped.reshape(b.shape[:-3] + (2 * size, b.shape[-1])))
    return jnp.stack([real, imag], -3)


def taylor_propagators(ham):
    size = ham.shape[-1]
    eye = jnp.eye(size, dtype=jnp.float32)
    gen = jnp.stack([ham[:, 1], -ham[:, 0]], 1)
    gen2 = cmul(gen, gen, taylor_mode)
    both = cmul(jnp.stack([gen, gen2], 0), gen2[None], taylor_mode)
    gen3, gen4 = both[0], both[1]
    coef = [1.0]
    for order in range(1, TAYLOR + 1):
        coef.append(coef[-1] / order)
    low = coef[1] * gen + coef[2] * gen2 + coef[3] * gen3
    low = low.at[:, 0].add(coef[0] * eye)
    high = coef[5] * gen + coef[6] * gen2 + coef[7] * gen3 + coef[8] * gen4
    high = high.at[:, 0].add(coef[4] * eye)
    return low + cmul(gen4, high, taylor_mode)


def shards(amplitudes, drift, controls, target):
    size = drift.shape[-1]
    tm_count = lax.axis_size("tm")
    tm_index = lax.axis_index("tm")
    col_count = lax.axis_size("col")
    col_width = size // col_count
    col_start = lax.axis_index("col") * col_width
    local_count = amplitudes.shape[1]
    exact = lax.Precision.HIGHEST

    raw = drift[None] + jnp.sum(amplitudes[:, :, None, None, None] * controls[:, None], axis=0)
    ham = jnp.stack(
        [0.5 * (raw[:, 0] + jnp.swapaxes(raw[:, 0], 1, 2)), 0.5 * (raw[:, 1] - jnp.swapaxes(raw[:, 1], 1, 2))], 1
    )
    steps = taylor_propagators(ham)

    running = [steps[0]]
    for position in range(1, local_count):
        running.append(cmul(steps[position][None], running[-1][None])[0])
    block_total = running[-1]
    split = 2 if col_count % 2 == 0 else 1
    part = lax.axis_index("col") % split
    rows = size // split
    mine = lax.dynamic_slice_in_dim(block_total, part * rows, rows, 1)
    if tm_count <= 8:
        received = []
        for shift in range(1, tm_count):
            pairs = [(i, (i + shift) % tm_count) for i in range(tm_count)]
            received.append(lax.ppermute(mine, "tm", pairs))
        received = jnp.stack(received, 0)
        if split == 2:
            theirs = lax.ppermute(received, "col", [(i, i ^ 1) for i in range(col_count)])
            own_block = block_total
            joined = jnp.zeros(received.shape[:2] + (size,) + received.shape[3:], received.dtype)
            joined = lax.dynamic_update_slice_in_dim(joined, received, part * rows, 2)
            received = lax.dynamic_update_slice_in_dim(joined, theirs, (1 - part) * rows, 2)
        else:
            own_block = block_total
        slots = jnp.arange(tm_count)[:, None, None, None]
        pieces = jnp.where(slots == tm_index, own_block[None], jnp.zeros_like(own_block)[None])
        for shift in range(1, tm_count):
            pieces = jnp.where(slots == (tm_index - shift) % tm_count, received[shift - 1][None], pieces)
    else:
        gathered = lax.all_gather(mine, "tm")
        if split == 2:
            theirs = lax.ppermute(gathered, "col", [(i, i ^ 1) for i in range(col_count)])
            upper = jnp.where(part == 0, gathered, theirs)
            lower = jnp.where(part == 0, theirs, gathered)
            pieces = jnp.concatenate([upper, lower], 2)
        else:
            pieces = gathered

    eye = jnp.eye(size, dtype=jnp.float32)
    start_full = jnp.stack([eye, jnp.zeros_like(eye)])
    if tm_count == 4:
        pairs = cmul(pieces[1::2], pieces[0::2])
        ends = cmul(jnp.stack([pairs[1], pieces[2]], 0), pairs[0][None])
        final_state = ends[0]
        options = jnp.stack([start_full, pieces[0], pairs[0], ends[1]], 0)
        prefix = lax.dynamic_index_in_dim(options, tm_index, 0, keepdims=False)
    elif tm_count <= 8:
        scan = pieces
        shift = 1
        while shift < tm_count:
            later = cmul(scan[shift:], scan[:-shift])
            scan = jnp.concatenate([scan[:shift], later], 0)
            shift *= 2
        final_state = scan[-1]
        earlier = lax.dynamic_index_in_dim(scan, jnp.maximum(tm_index - 1, 0), 0, keepdims=False)
        prefix = jnp.where(tm_index == 0, start_full, earlier)
    else:

        def lap(carry, piece):
            total, prefix, position = carry
            prefix = jnp.where(position == tm_index, total, prefix)
            total = cmul(piece[None], total[None])[0]
            return (total, prefix, position + 1), None

        (final_state, prefix, _), _ = lax.scan(lap, (start_full, start_full, 0), pieces)
    states = cmul(jnp.stack(running, 0), prefix[None])
    overlap = cmul_adjoint_left(target, final_state)

    correlation_real = jnp.sum(target[0] * final_state[0] + target[1] * final_state[1])
    correlation_imag = jnp.sum(target[0] * final_state[1] - target[1] * final_state[0])
    weighted = cmul_adjoint_right(cmul(states, overlap[None]), states)
    control_real = (0.5 * (controls[:, 0] + jnp.swapaxes(controls[:, 0], 1, 2)))[:, None]
    control_imag = (0.5 * (controls[:, 1] - jnp.swapaxes(controls[:, 1], 1, 2)))[:, None]
    trace_real = jnp.sum(control_real * weighted[None, :, 0] + control_imag * weighted[None, :, 1], axis=(2, 3))
    trace_imag = jnp.sum(control_real * weighted[None, :, 1] - control_imag * weighted[None, :, 0], axis=(2, 3))
    gradient = correlation_real * trace_imag - correlation_imag * trace_real
    propagators = cmul(jnp.stack(running, 0), lax.dynamic_slice_in_dim(prefix, col_start, col_width, 2)[None])
    return (gradient, propagators)


def solution(mesh):
    in_specs = (P("grp", "tm"), P(), P(), P("grp", None, None))
    out_specs = (P("grp", "tm"), P(("grp", "tm"), None, None, "col"))
    return jax.shard_map(shards, mesh=mesh, in_specs=in_specs, out_specs=out_specs, check_vma=False)
```

```python
import jax
import jax.numpy as jnp
from jax import lax
from jax.sharding import PartitionSpec as P

TAYLOR = 8

fast_mode = lax.Precision.HIGHEST
taylor_mode = lax.Precision.HIGHEST


def mm(left, right, mode=fast_mode):
    return jnp.matmul(left, right, precision=mode)


def mm_nt(left, right):
    return jnp.einsum("...ij,...kj->...ik", left, right, precision=fast_mode)


def mm_tn(left, right):
    return jnp.einsum("...ji,...jk->...ik", left, right, precision=fast_mode)


def cmul(a, b, mode=fast_mode):
    size = a.shape[-2]
    stacked = a.reshape(a.shape[:-3] + (2 * size, a.shape[-1]))
    with_real = mm(stacked, b[..., 0, :, :], mode)
    with_imag = mm(stacked, b[..., 1, :, :], mode)
    real = with_real[..., :size, :] - with_imag[..., size:, :]
    imag = with_imag[..., :size, :] + with_real[..., size:, :]
    return jnp.stack([real, imag], -3)


def cmul_adjoint_right(a, b):
    size = a.shape[-2]
    stacked = a.reshape(a.shape[:-3] + (2 * size, a.shape[-1]))
    with_real = mm_nt(stacked, b[..., 0, :, :])
    with_imag = mm_nt(stacked, b[..., 1, :, :])
    real = with_real[..., :size, :] + with_imag[..., size:, :]
    imag = with_real[..., size:, :] - with_imag[..., :size, :]
    return jnp.stack([real, imag], -3)


def cmul_adjoint_left(a, b):
    size = a.shape[-2]
    stacked = a.reshape(a.shape[:-3] + (2 * size, a.shape[-1]))
    real = mm_tn(stacked, b.reshape(b.shape[:-3] + (2 * size, b.shape[-1])))
    swapped = jnp.stack([b[..., 1, :, :], -b[..., 0, :, :]], -3)
    imag = mm_tn(stacked, swapped.reshape(b.shape[:-3] + (2 * size, b.shape[-1])))
    return jnp.stack([real, imag], -3)


def taylor_propagators(ham):
    size = ham.shape[-1]
    eye = jnp.eye(size, dtype=jnp.float32)
    gen = jnp.stack([ham[:, 1], -ham[:, 0]], 1)
    gen2 = cmul(gen, gen, taylor_mode)
    both = cmul(jnp.stack([gen, gen2], 0), gen2[None], taylor_mode)
    gen3, gen4 = both[0], both[1]
    coef = [1.0]
    for order in range(1, TAYLOR + 1):
        coef.append(coef[-1] / order)
    low = coef[1] * gen + coef[2] * gen2 + coef[3] * gen3
    low = low.at[:, 0].add(coef[0] * eye)
    high = coef[5] * gen + coef[6] * gen2 + coef[7] * gen3 + coef[8] * gen4
    high = high.at[:, 0].add(coef[4] * eye)
    return low + cmul(gen4, high, taylor_mode)


def shards(amplitudes, drift, controls, target):
    size = drift.shape[-1]
    tm_count = lax.axis_size("tm")
    tm_index = lax.axis_index("tm")
    col_count = lax.axis_size("col")
    col_width = size // col_count
    col_start = lax.axis_index("col") * col_width
    local_count = amplitudes.shape[1]
    exact = lax.Precision.HIGHEST

    raw = drift[None] + jnp.sum(amplitudes[:, :, None, None, None] * controls[:, None], axis=0)
    ham = jnp.stack(
        [0.5 * (raw[:, 0] + jnp.swapaxes(raw[:, 0], 1, 2)), 0.5 * (raw[:, 1] - jnp.swapaxes(raw[:, 1], 1, 2))], 1
    )
    steps = taylor_propagators(ham)

    running = [steps[0]]
    for position in range(1, local_count):
        running.append(cmul(steps[position][None], running[-1][None])[0])
    block_total = running[-1]
    split = 2 if col_count % 2 == 0 else 1
    part = lax.axis_index("col") % split
    rows = size // split
    mine = lax.dynamic_slice_in_dim(block_total, part * rows, rows, 1)
    if tm_count <= 8:
        received = []
        for shift in range(1, tm_count):
            pairs = [(i, (i + shift) % tm_count) for i in range(tm_count)]
            received.append(lax.ppermute(mine, "tm", pairs))
        received = jnp.stack(received, 0)
        if split == 2:
            theirs = lax.ppermute(received, "col", [(i, i ^ 1) for i in range(col_count)])
            own_block = block_total
            joined = jnp.zeros(received.shape[:2] + (size,) + received.shape[3:], received.dtype)
            joined = lax.dynamic_update_slice_in_dim(joined, received, part * rows, 2)
            received = lax.dynamic_update_slice_in_dim(joined, theirs, (1 - part) * rows, 2)
        else:
            own_block = block_total
        slots = jnp.arange(tm_count)[:, None, None, None]
        pieces = jnp.where(slots == tm_index, own_block[None], jnp.zeros_like(own_block)[None])
        for shift in range(1, tm_count):
            pieces = jnp.where(slots == (tm_index - shift) % tm_count, received[shift - 1][None], pieces)
    else:
        gathered = lax.all_gather(mine, "tm")
        if split == 2:
            theirs = lax.ppermute(gathered, "col", [(i, i ^ 1) for i in range(col_count)])
            upper = jnp.where(part == 0, gathered, theirs)
            lower = jnp.where(part == 0, theirs, gathered)
            pieces = jnp.concatenate([upper, lower], 2)
        else:
            pieces = gathered

    eye = jnp.eye(size, dtype=jnp.float32)
    start_full = jnp.stack([eye, jnp.zeros_like(eye)])
    if tm_count == 4:
        pairs = cmul(pieces[1::2], pieces[0::2])
        ends = cmul(jnp.stack([pairs[1], pieces[2]], 0), pairs[0][None])
        final_state = ends[0]
        options = jnp.stack([start_full, pieces[0], pairs[0], ends[1]], 0)
        prefix = lax.dynamic_index_in_dim(options, tm_index, 0, keepdims=False)
    elif tm_count <= 8:
        scan = pieces
        shift = 1
        while shift < tm_count:
            later = cmul(scan[shift:], scan[:-shift])
            scan = jnp.concatenate([scan[:shift], later], 0)
            shift *= 2
        final_state = scan[-1]
        earlier = lax.dynamic_index_in_dim(scan, jnp.maximum(tm_index - 1, 0), 0, keepdims=False)
        prefix = jnp.where(tm_index == 0, start_full, earlier)
    else:

        def lap(carry, piece):
            total, prefix, position = carry
            prefix = jnp.where(position == tm_index, total, prefix)
            total = cmul(piece[None], total[None])[0]
            return (total, prefix, position + 1), None

        (final_state, prefix, _), _ = lax.scan(lap, (start_full, start_full, 0), pieces)
    states = cmul(jnp.stack(running, 0), prefix[None])
    overlap = cmul_adjoint_left(target, final_state)

    correlation_real = jnp.sum(target[0] * final_state[0] + target[1] * final_state[1])
    correlation_imag = jnp.sum(target[0] * final_state[1] - target[1] * final_state[0])
    weighted = cmul_adjoint_right(cmul(states, overlap[None]), states)
    control_real = (0.5 * (controls[:, 0] + jnp.swapaxes(controls[:, 0], 1, 2)))[:, None]
    control_imag = (0.5 * (controls[:, 1] - jnp.swapaxes(controls[:, 1], 1, 2)))[:, None]
    partial_real = jnp.sum(control_real * weighted[None, :, 0] + control_imag * weighted[None, :, 1], axis=2)
    partial_imag = jnp.sum(control_real * weighted[None, :, 1] - control_imag * weighted[None, :, 0], axis=2)
    partial_real, partial_imag = lax.optimization_barrier((partial_real, partial_imag))
    trace_real = jnp.sum(partial_real, axis=-1)
    trace_imag = jnp.sum(partial_imag, axis=-1)
    gradient = correlation_real * trace_imag - correlation_imag * trace_real
    propagators = cmul(jnp.stack(running, 0), lax.dynamic_slice_in_dim(prefix, col_start, col_width, 2)[None])
    return (gradient, propagators)


def solution(mesh):
    in_specs = (P("grp", "tm"), P(), P(), P("grp", None, None))
    out_specs = (P("grp", "tm"), P(("grp", "tm"), None, None, "col"))
    return jax.shard_map(shards, mesh=mesh, in_specs=in_specs, out_specs=out_specs, check_vma=False)
```
